32 devices in a mesh: dp: 16 (over z, y, x), ctx: 2 (over core).
Axes of the slice: x: 2, y: 2, z: 4, core: 2. Of those that a mesh axis runs over, the one named last changes fastest.
Arguments:
- inputs: bfloat16 [16, 1024, 1024], P('dp', 'ctx'), may hold values from -6 to 6
- teacher: bfloat16 [16, 1024, 1024], P('dp', 'ctx'), may hold values from -6 to 6
- valid_mask: int32 [16, 1024], P('dp', 'ctx'), may hold values from 0 to 1, as said below
- token_types: int32 [16, 1024], P('dp', 'ctx'), may hold values from 0 to 2
- type_table: bfloat16 [3, 1024], P(None, ('dp', 'ctx')), may hold values from -3 to 3
- first_gain: bfloat16 [1024], P(('dp', 'ctx')), may hold values from 0.099609375 to 1.8984375
- first_shift: bfloat16 [1024], P(('dp', 'ctx')), may hold values from -2 to 2
- input_proj: bfloat16 [1024, 3072], P(('dp', 'ctx')), may hold values from -0.25 to 0.25
- output_proj: bfloat16 [1024, 1024], P(('dp', 'ctx')), may hold values from -1.5 to 1.5
- output_bias: bfloat16 [1024], P(('dp', 'ctx')), may hold values from -2 to 2
- second_gain: bfloat16 [1024], P(('dp', 'ctx')), may hold values from 0.099609375 to 1.8984375
- second_shift: bfloat16 [1024], P(('dp', 'ctx')), may hold values from -2 to 2
- up_proj: bfloat16 [1024, 4096], P(('dp', 'ctx')), may hold values from -0.1875 to 0.1875
- up_bias: bfloat16 [4096], P(('dp', 'ctx')), may hold values from -2 to 2
- down_proj: bfloat16 [4096, 1024], P(('dp', 'ctx')), may hold values from -0.09375 to 0.09375
- down_bias: bfloat16 [1024], P(('dp', 'ctx')), may hold values from -2 to 2
Outputs:
- activations: float32 [16, 1024, 1024], P('dp', 'ctx')
- loss: float32 [], replicated
- grad_inputs: float32 [16, 1024, 1024], P('dp', 'ctx')
- grad_table: float32 [3, 1024], P(None, ('dp', 'ctx'))
- grad_first_gain: float32 [1024], P(('dp', 'ctx'))
- grad_first_shift: float32 [1024], P(('dp', 'ctx'))
- grad_input_proj: float32 [1024, 3072], P(('dp', 'ctx'))
- grad_output_proj: float32 [1024, 1024], P(('dp', 'ctx'))
- grad_output_bias: float32 [1024], P(('dp', 'ctx'))
- grad_second_gain: float32 [1024], P(('dp', 'ctx'))
- grad_second_shift: float32 [1024], P(('dp', 'ctx'))
- grad_up_proj: float32 [1024, 4096], P(('dp', 'ctx'))
- grad_up_bias: float32 [4096], P(('dp', 'ctx'))
- grad_down_proj: float32 [4096, 1024], P(('dp', 'ctx'))
- grad_down_bias: float32 [1024], P(('dp', 'ctx'))
The draws below stay inside these ranges and needn't reach their ends.
Inputs may be any that keep to these rules, and one draw needn't show every extreme that they name: `valid_mask`: 1 marks a token that the loss counts.
All inputs are finite; a program needn't handle non-finite values.
Results may differ from the reference program's by a relative error of at most 0.013.
Values may be sent and summed in bfloat16 or wider, within the bound.
No kernel may reach another device: no remote copies, remote signals or barrier semaphores. Data moves between devices by JAX's collectives and lax.ppermute only.
A program may use at most 192 MiB of HBM per device.

```python
import math
import jax
import jax.numpy as jnp
from jax import lax

D = 1024
HEADS = 16
HEAD_DIM = 64
FF = 4096
TYPES = 3
LEN = 1024
BATCH = 16
TOKENS = 16384


def draw_valid_mask(key, part):
    total_rows = BATCH * LEN
    position = jnp.arange(total_rows, dtype=jnp.int32)
    thresholds = 250 + 7 * (position * 100 // total_rows)
    samples = jax.random.randint(key, (total_rows,), 0, 1000, dtype=jnp.int32)
    return (samples < thresholds).astype(jnp.int32).reshape(BATCH, LEN)


def with_ends(drawn, key, smallest, high):
    longest = drawn.shape.index(max(drawn.shape))
    spots = []
    for shift in (0, 1):
        where = [jax.random.randint(jax.random.fold_in(key, axis), (), 0, length) for axis, length in enumerate(drawn.shape)]
        where[longest] = (where[longest] + shift) % drawn.shape[longest]
        spots.append(tuple(where))
    return drawn.at[spots[0]].set(smallest).at[spots[1]].set(high)


def block_levels(key, shape, pieces, smallest, largest):
    def one(dim, shards_of):
        heights = jax.random.uniform(jax.random.fold_in(jax.random.fold_in(key, 6), dim), (shards_of,), jnp.float32, smallest / len(pieces), largest / len(pieces))
        return jnp.repeat(jnp.exp(heights), shape[dim] // shards_of).reshape((-1,) + (1,) * (len(shape) - dim - 1))

    loudness = one(*pieces[0])
    for cut in pieces[1:]:
        loudness = loudness * one(*cut)
    return loudness


def noise(own_key, dims, scale, reach, shards=(), held_as=jnp.bfloat16):
    values = jax.random.normal(own_key, dims, jnp.float32) * scale
    if len(shards) > 0:
        values = block_levels(own_key, dims, shards, -0.22, 0.18) * values
    return jnp.clip(values, min=-reach, max=reach).astype(held_as)


def setup_inputs(seed: int = 0) -> dict:
    splits = jax.random.split(jax.random.key(seed), 17)
    inputs = noise(splits[0], (BATCH, LEN, D), 1.0, 6.0, ((0, 16), (1, 2)))
    teacher = noise(splits[1], (BATCH, LEN, D), 1.0, 6.0, ((0, 16), (1, 2)))
    valid_mask = draw_valid_mask(jax.random.fold_in(splits[16], 71), 0)
    token_types = with_ends(jax.random.randint(splits[3], (BATCH, LEN), 0, TYPES), jax.random.fold_in(splits[3], 1), 0, TYPES - 1).astype(jnp.int32)
    type_table = noise(splits[4], (TYPES, D), 0.5, 3.0, ((1, 32),))
    first_gain = jnp.clip(1.0 + 0.18 * jax.random.normal(splits[5], (D,), jnp.float32), 0.099609375, 1.8984375).astype(jnp.bfloat16)
    first_shift = noise(splits[6], (D,), 0.3, 2.0, ((0, 32),))
    input_proj = noise(splits[7], (D, 3 * D), (D // 2) ** -0.5, 0.25, ((0, 32),))
    output_proj = noise(splits[8], (D, D), (D // 64) ** -0.5, 1.5, ((0, 32),))
    output_bias = noise(splits[9], (D,), 0.3, 2.0, ((0, 32),))
    second_gain = jnp.clip(1.0 + 0.18 * jax.random.normal(splits[10], (D,), jnp.float32), 0.099609375, 1.8984375).astype(jnp.bfloat16)
    second_shift = noise(splits[11], (D,), 0.3, 2.0, ((0, 32),))
    up_proj = noise(splits[12], (D, FF), D ** -0.5, 0.1875, ((0, 32),))
    up_bias = noise(splits[13], (FF,), 0.3, 2.0, ((0, 32),))
    down_proj = noise(splits[14], (FF, D), FF ** -0.5, 0.09375, ((0, 32),))
    down_bias = noise(splits[15], (D,), 0.3, 2.0, ((0, 32),))
    return dict(inputs=inputs, teacher=teacher, valid_mask=valid_mask, token_types=token_types, type_table=type_table, first_gain=first_gain, first_shift=first_shift, input_proj=input_proj, output_proj=output_proj, output_bias=output_bias, second_gain=second_gain, second_shift=second_shift, up_proj=up_proj, up_bias=up_bias, down_proj=down_proj, down_bias=down_bias)


@jax.custom_vjp
def low(v):
    return lax.optimization_barrier(v.astype(jnp.bfloat16)).astype(jnp.float32)

@jax.custom_vjp
def low_back(v):
    return v

def low_keep(v):
    return (low(v), None)

def low_pass(kept, grad):
    return (grad,)

def back_keep(v):
    return (v, None)

def back_low(kept, grad):
    return (low(grad),)
low.defvjp(low_keep, low_pass)
low_back.defvjp(back_keep, back_low)
EPSILON = 1e-05
HIGHEST = lax.Precision.HIGHEST

def layer_norm(values, norm_gain, norm_shift):
    centre = values - lax.optimization_barrier(jnp.mean(values, axis=-1, keepdims=True))
    spread = lax.optimization_barrier(jnp.mean(centre * centre, axis=-1, keepdims=True))
    return centre * lax.rsqrt(spread + EPSILON) * norm_gain + norm_shift

def matmul_high(left, right):
    return jnp.dot(left, right, precision=HIGHEST)

def attend_sequence(queries, key_rows, value_rows):
    query_rows = math.gcd(LEN, 512)
    score_scale = HEAD_DIM ** (-0.5)

    def per_block(query_block):
        scores = low_back(jnp.einsum('qhd,khd->qhk', query_block, key_rows, precision=HIGHEST) * score_scale)
        weights = low(jax.nn.softmax(scores, axis=-1))
        return jnp.einsum('qhk,khd->qhd', weights, value_rows, precision=HIGHEST)
    blocks = queries.reshape(LEN // query_rows, query_rows, HEADS, HEAD_DIM)
    return lax.map(jax.checkpoint(per_block), blocks).reshape(LEN, HEADS * HEAD_DIM)

def sequence_forward(params, row_in, type_row):
    type_rows, gain_one, shift_one, proj_in, proj_out, bias_out, gain_two, shift_two, proj_up, bias_up, proj_down, bias_down = params
    onehot = (type_row[:, None] == jnp.arange(TYPES, dtype=jnp.int32)[None, :]).astype(row_in.dtype)
    hidden = row_in + matmul_high(onehot, type_rows)
    normed_one = low(layer_norm(hidden, gain_one, shift_one))
    projected = low(low_back(matmul_high(normed_one, proj_in)))
    queries = projected[:, :D].reshape(LEN, HEADS, HEAD_DIM)
    key_rows = projected[:, D:2 * D].reshape(LEN, HEADS, HEAD_DIM)
    value_rows = projected[:, 2 * D:].reshape(LEN, HEADS, HEAD_DIM)
    attended = low(low_back(attend_sequence(queries, key_rows, value_rows)))
    after_attn = hidden + low_back(matmul_high(attended, proj_out) + bias_out)
    normed_two = low(layer_norm(after_attn, gain_two, shift_two))
    pre_act = low_back(matmul_high(normed_two, proj_up) + bias_up)
    activ = low(jax.nn.gelu(pre_act, approximate=False))
    return after_attn + low_back(matmul_high(activ, proj_down) + bias_down)

def reference(inputs, teacher, valid_mask, token_types, type_table, first_gain, first_shift, input_proj, output_proj, output_bias, second_gain, second_shift, up_proj, up_bias, down_proj, down_bias):
    params = tuple((weight_arg.astype(jnp.float32) for weight_arg in (type_table, first_gain, first_shift, input_proj, output_proj, output_bias, second_gain, second_shift, up_proj, up_bias, down_proj, down_bias)))
    inputs_f = inputs.astype(jnp.float32)
    teacher_f = teacher.astype(jnp.float32)
    mask_f = valid_mask.astype(jnp.float32)
    valid_total = jnp.sum(mask_f)

    def whole_layer(params_in, inputs_in):

        def per_seq(carried, packed):
            row_in, type_row, target, keep_rows = packed
            result = jax.checkpoint(sequence_forward)(params_in, row_in, type_row)
            error_rows = result - target
            return (carried + jnp.sum(keep_rows[:, None] * error_rows * error_rows), result)
        loss_total, results = lax.scan(per_seq, jnp.zeros((), jnp.float32), (inputs_in, token_types, teacher_f, mask_f))
        return (results, loss_total / (valid_total * D))
    (results, loss_value), pullback = jax.vjp(whole_layer, params, inputs_f)
    cotangent = (jnp.zeros_like(results), jnp.asarray(TOKENS * D, dtype=loss_value.dtype))
    grads_params, grad_inputs = pullback(cotangent)
    return (results, loss_value, grad_inputs, grads_params[0], grads_params[1], grads_params[2], grads_params[3], grads_params[4], grads_params[5], grads_params[6], grads_params[7], grads_params[8], grads_params[9], grads_params[10], grads_params[11])
```

```python
import numpy as np

import jax
import jax.numpy as jnp
from jax import lax
from jax.sharding import PartitionSpec as P

HEADS = 16
TYPES = 3


EPSILON = 1e-05


def layer_norm(values, norm_gain, norm_shift):
    centre = values - jnp.mean(values, axis=-1, keepdims=True)
    spread = jnp.mean(centre * centre, axis=-1, keepdims=True)
    return centre * lax.rsqrt(spread + EPSILON) * norm_gain + norm_shift


def gelu_exact(values):
    return jax.nn.gelu(values, approximate=False)


def split_blocks(tensor, head_count):
    batch_size, length, width_all = tensor.shape
    block_size = length
    shaped = tensor.reshape(
        batch_size, length // block_size, block_size, head_count, width_all // head_count
    )
    return jnp.moveaxis(shaped, 1, 0)


def attend_piece(queries, score_scale, carried, arrived):
    key_rows, value_rows = arrived
    head_count = queries.shape[2]
    key_blocks = split_blocks(key_rows, head_count)
    value_blocks = split_blocks(value_rows, head_count)

    def online_step(running, block_pair):
        run_max, run_sum, accumulated = running
        key_block, value_block = block_pair
        scores = (
            jnp.einsum("bqhd,bkhd->bqhk", queries, key_block, preferred_element_type=jnp.float32)
            * score_scale
        )
        new_max = jnp.maximum(run_max, jnp.max(scores, axis=-1))
        factor = jnp.exp(run_max - new_max)
        weights = jnp.exp(scores - new_max[..., None])
        run_sum = run_sum * factor + jnp.sum(weights, axis=-1)
        accumulated = accumulated * factor[..., None] + jnp.einsum(
            "bqhk,bkhd->bqhd",
            weights.astype(jnp.bfloat16),
            value_block,
            preferred_element_type=jnp.float32,
        )
        return ((new_max, run_sum, accumulated), None)

    carried, unused = lax.scan(online_step, carried, (key_blocks, value_blocks))
    return carried


def backward_keys(queries, grad_attended, log_total, delta_rows, score_scale, key_all, value_all):
    head_count = queries.shape[2]
    key_blocks = split_blocks(key_all, head_count)
    value_blocks = split_blocks(value_all, head_count)

    def back_step(grad_query, block_pair):
        key_block, value_block = block_pair
        scores = (
            jnp.einsum("bqhd,bkhd->bqhk", queries, key_block, preferred_element_type=jnp.float32)
            * score_scale
        )
        probs = jnp.exp(scores - log_total[..., None])
        grad_probs = jnp.einsum(
            "bqhd,bkhd->bqhk", grad_attended, value_block, preferred_element_type=jnp.float32
        )
        grad_scores = (probs * (grad_probs - delta_rows[..., None])).astype(jnp.bfloat16)
        grad_query = (
            grad_query
            + jnp.einsum(
                "bqhk,bkhd->bqhd", grad_scores, key_block, preferred_element_type=jnp.float32
            )
            * score_scale
        )
        grad_key = (
            jnp.einsum("bqhk,bqhd->bkhd", grad_scores, queries, preferred_element_type=jnp.float32)
            * score_scale
        )
        grad_value = jnp.einsum(
            "bqhk,bqhd->bkhd",
            probs.astype(jnp.bfloat16),
            grad_attended,
            preferred_element_type=jnp.float32,
        )
        return (grad_query, (grad_key, grad_value))

    initial = jnp.zeros(queries.shape, jnp.float32)
    grad_query, (key_parts, value_parts) = lax.scan(back_step, initial, (key_blocks, value_blocks))
    batch_size, length = (key_all.shape[0], key_all.shape[1])
    grad_keys = jnp.moveaxis(key_parts, 0, 1).reshape(batch_size, length, -1)
    grad_values = jnp.moveaxis(value_parts, 0, 1).reshape(batch_size, length, -1)
    return (grad_query, grad_keys, grad_values)


def dp_subaxes(mesh):
    devs = np.asarray(mesh.devices)
    n_dp = devs.shape[0]
    single = ((n_dp, 1),)
    try:
        coords = [tuple(int(v) for v in d.coords) for d in devs[:, 0]]
    except Exception:
        return single
    rank = len(coords[0])
    subs = []
    stride = 1
    while stride < n_dp:
        diff = [k for k in range(rank) if coords[stride][k] != coords[0][k]]
        if len(diff) != 1 or n_dp % stride:
            return single
        axis = diff[0]
        size = 1
        while size * stride < n_dp:
            here = coords[size * stride]
            same_rest = all(here[k] == coords[0][k] for k in range(rank) if k != axis)
            if here[axis] == coords[0][axis] or not same_rest:
                break
            size += 1
        if n_dp % (stride * size):
            return single
        subs.append((size, stride))
        stride *= size
    if stride != n_dp:
        return single
    return tuple(subs)


def _ring_perm(n_axis, size, stride):
    pairs = []
    for i in range(n_axis):
        digit = (i // stride) % size
        pairs.append((i, i + (((digit + 1) % size) - digit) * stride))
    return pairs


def _digit(me, size, stride):
    return (me // stride) % size


def _ring_rs(block_of, n, me, axis, perm):
    if n == 1:
        return block_of(0)
    acc = block_of((me + n - 1) % n)
    for step in range(n - 1):
        acc = lax.ppermute(acc, axis, perm) + block_of((me + 2 * n - 2 - step) % n)
    return acc


def _ring_ag(piece, n, me, axis, perm, dim):
    if n == 1:
        return jnp.expand_dims(piece, dim)
    out = jnp.zeros(piece.shape[:dim] + (n,) + piece.shape[dim:], piece.dtype)
    out = lax.dynamic_update_index_in_dim(out, piece, me, dim)
    cur = piece
    for step in range(1, n):
        cur = lax.ppermute(cur, axis, perm)
        out = lax.dynamic_update_index_in_dim(out, cur, (me + n - step) % n, dim)
    return out


class Rings:
    def __init__(self, subs, n_dp, n_ctx):
        self.subs = subs
        self.n_dp = n_dp
        self.n_ctx = n_ctx
        self.dp_perms = [_ring_perm(n_dp, size, stride) for size, stride in subs]
        self.ctx_perm = _ring_perm(n_ctx, n_ctx, 1)
        order = sorted(range(len(subs)), key=lambda k: subs[k][0])
        swapped = list(order)
        if len(swapped) >= 2:
            swapped[0], swapped[1] = swapped[1], swapped[0]
        self.rs_orders = (order, swapped)
        self.me_dp = lax.axis_index("dp")
        self.me_ctx = lax.axis_index("ctx")

    def _col_parts(self, width, colors):
        if colors > 1 and width % (128 * colors) == 0:
            step = width // colors
            return [(k * step, (k + 1) * step) for k in range(colors)]
        return [(0, width)]

    def gather(self, shard, colors=2):
        rows, width = shard.shape
        pieces = []
        for color, (c0, c1) in enumerate(self._col_parts(width, colors)):
            part = shard[:, c0:c1]
            done = []
            for k in reversed(self.rs_orders[color % 2]):
                size, stride = self.subs[k]
                pos = sum(1 for g in done if g > k)
                part = _ring_ag(
                    part, size, _digit(self.me_dp, size, stride), "dp", self.dp_perms[k], pos
                )
                done.append(k)
            part = part.reshape((self.n_dp, rows, c1 - c0))
            part = _ring_ag(part, self.n_ctx, self.me_ctx, "ctx", self.ctx_perm, 1)
            pieces.append(part.reshape((self.n_dp * self.n_ctx * rows, c1 - c0)))
        if len(pieces) == 1:
            return pieces[0]
        return jnp.concatenate(pieces, axis=1)

    def scatter(self, block_of, rows, width, colors=2):
        pieces = []
        for color, (c0, c1) in enumerate(self._col_parts(width, colors)):
            acc = _ring_rs(
                lambda b, c0=c0, c1=c1: block_of(b, c0, c1),
                self.n_ctx,
                self.me_ctx,
                "ctx",
                self.ctx_perm,
            )
            shape = tuple(size for size, _ in reversed(self.subs)) + (rows, c1 - c0)
            acc = acc.reshape(shape)
            left = list(range(len(self.subs)))
            for k in self.rs_orders[color % 2]:
                size, stride = self.subs[k]
                pos = sum(1 for g in left if g > k)
                cur = acc
                acc = _ring_rs(
                    lambda b, cur=cur, pos=pos: lax.dynamic_index_in_dim(
                        cur, b, pos, keepdims=False
                    ),
                    size,
                    _digit(self.me_dp, size, stride),
                    "dp",
                    self.dp_perms[k],
                )
                left.remove(k)
            pieces.append(acc)
        if len(pieces) == 1:
            return pieces[0]
        return jnp.concatenate(pieces, axis=1)

    def ctx_gather_rows(self, piece):
        out = _ring_ag(piece, self.n_ctx, self.me_ctx, "ctx", self.ctx_perm, 0)
        return out.reshape((-1,) + piece.shape[1:])

    def ctx_scatter_rows(self, full):
        shaped = full.reshape((self.n_ctx, -1) + full.shape[1:])
        return _ring_rs(
            lambda b: lax.dynamic_index_in_dim(shaped, b, 0, keepdims=False),
            self.n_ctx,
            self.me_ctx,
            "ctx",
            self.ctx_perm,
        )


def _ctx_block_cols(values, n_dp, n_ctx, rows, b):
    tok = values.shape[0]
    shaped = values.reshape(tok, n_dp, n_ctx, rows)
    return lax.dynamic_index_in_dim(shaped, b, 2, keepdims=False).reshape(tok, n_dp * rows)


def body(
    subs,
    inputs,
    teacher,
    valid_mask,
    token_types,
    type_table,
    first_gain,
    first_shift,
    input_proj,
    output_proj,
    output_bias,
    second_gain,
    second_shift,
    up_proj,
    up_bias,
    down_proj,
    down_bias,
):
    batch_size, tok_rows, width_all = inputs.shape
    row_count = batch_size * tok_rows
    head_count = HEADS
    head_dim = width_all // head_count
    score_scale = head_dim ** (-0.5)
    n_dp = lax.axis_size("dp")
    n_ctx = lax.axis_size("ctx")
    rings = Rings(subs, n_dp, n_ctx)
    shard_rows = first_gain.shape[0]
    ff_all = up_proj.shape[1]
    ff_per_row = ff_all // width_all
    mask_rows = valid_mask.reshape(row_count).astype(jnp.float32)

    count = jnp.sum(valid_mask)
    first_row = (jnp.arange(shard_rows) == 0)[:, None]
    count_cols = jnp.where(
        first_row,
        jnp.stack([count // 16, count % 16]).astype(jnp.bfloat16)[None, :],
        jnp.zeros((1, 2), jnp.bfloat16),
    )
    small = jnp.concatenate(
        [
            type_table.T,
            jnp.stack(
                [first_gain, first_shift, output_bias, second_gain, second_shift, down_bias],
                axis=1,
            ),
            up_bias.reshape(shard_rows, ff_per_row),
            count_cols,
        ],
        axis=1,
    )
    small_all = rings.gather(small, colors=1).astype(jnp.float32)
    table_full = small_all[:, 0:TYPES].T
    gain_one, shift_one, bias_out, gain_two, shift_two, bias_down = (
        small_all[:, TYPES + k] for k in range(6)
    )
    bias_up = small_all[:, TYPES + 6 : TYPES + 6 + ff_per_row].reshape(ff_all)
    count_at = TYPES + 6 + ff_per_row
    valid_total = jnp.sum(small_all[:, count_at]) * 16.0 + jnp.sum(small_all[:, count_at + 1])

    proj_in = rings.gather(input_proj)
    proj_out = rings.gather(output_proj)
    proj_up = rings.gather(up_proj)
    proj_down = rings.gather(down_proj)

    onehot = (
        token_types.reshape(row_count)[:, None] == jnp.arange(TYPES, dtype=jnp.int32)[None, :]
    ).astype(jnp.float32)
    hidden = inputs.reshape(row_count, width_all).astype(jnp.float32) + jnp.dot(
        onehot, table_full, precision=lax.Precision.HIGHEST
    )
    normed_one, norm_pull_one = jax.vjp(layer_norm, hidden, gain_one, shift_one)
    normed_one_low = normed_one.astype(jnp.bfloat16)
    projected = jnp.dot(normed_one_low, proj_in, preferred_element_type=jnp.float32).astype(
        jnp.bfloat16
    )
    queries = projected[:, :width_all].reshape(batch_size, tok_rows, head_count, head_dim)
    key_rows = projected[:, width_all : 2 * width_all]
    value_rows = projected[:, 2 * width_all :]
    key_all = rings.ctx_gather_rows(key_rows).reshape(batch_size, -1, width_all)
    value_all = rings.ctx_gather_rows(value_rows).reshape(batch_size, -1, width_all)
    start_state = (
        jnp.full((batch_size, tok_rows, head_count), -1e30, jnp.float32),
        jnp.zeros((batch_size, tok_rows, head_count), jnp.float32),
        jnp.zeros((batch_size, tok_rows, head_count, head_dim), jnp.float32),
    )
    running = attend_piece(queries, score_scale, start_state, (key_all, value_all))
    run_max, run_sum, accumulated = running
    attended_full = accumulated / run_sum[..., None]
    log_total = run_max + jnp.log(run_sum)
    attended_low = attended_full.reshape(row_count, width_all).astype(jnp.bfloat16)
    after_attn = (
        hidden
        + jnp.dot(attended_low, proj_out, preferred_element_type=jnp.float32)
        + bias_out
    )
    normed_two, norm_pull_two = jax.vjp(layer_norm, after_attn, gain_two, shift_two)
    normed_two_low = normed_two.astype(jnp.bfloat16)
    pre_act = jnp.dot(normed_two_low, proj_up, preferred_element_type=jnp.float32) + bias_up
    activ_full, gelu_pull = jax.vjp(gelu_exact, pre_act)
    activ_low = activ_full.astype(jnp.bfloat16)
    result = (
        after_attn
        + jnp.dot(activ_low, proj_down, preferred_element_type=jnp.float32)
        + bias_down
    )
    error_rows = result - teacher.reshape(row_count, width_all).astype(jnp.float32)
    local_square = jnp.sum(mask_rows[:, None] * error_rows * error_rows)
    rows_all = row_count * n_dp * n_ctx
    grad_act = 2.0 * rows_all / valid_total * mask_rows[:, None] * error_rows

    def weight_grad(left, right, rows):
        def block_of(b, c0, c1):
            return jnp.einsum(
                "rd,re->de",
                _ctx_block_cols(left, n_dp, n_ctx, rows, b),
                right[:, c0:c1],
                preferred_element_type=jnp.float32,
            )

        return rings.scatter(block_of, rows, right.shape[1])

    grad_branch_two = grad_act.astype(jnp.bfloat16)
    grad_down = weight_grad(activ_low, grad_branch_two, down_proj.shape[0])
    grad_down_bias = jnp.sum(grad_branch_two.astype(jnp.float32), axis=0)
    grad_activ = jnp.einsum(
        "rd,fd->rf", grad_branch_two, proj_down, preferred_element_type=jnp.float32
    )
    grad_pre = gelu_pull(grad_activ)[0].astype(jnp.bfloat16)
    grad_up = weight_grad(normed_two_low, grad_pre, up_proj.shape[0])
    grad_up_bias = jnp.sum(grad_pre.astype(jnp.float32), axis=0)
    grad_normed_two = jnp.einsum("rf,df->rd", grad_pre, proj_up, preferred_element_type=jnp.float32)
    grad_after_norm, grad_gain_two, grad_shift_two = norm_pull_two(grad_normed_two)
    grad_after = grad_act + grad_after_norm
    grad_branch_one = grad_after.astype(jnp.bfloat16)
    grad_out = weight_grad(attended_low, grad_branch_one, output_proj.shape[0])
    grad_out_bias = jnp.sum(grad_branch_one.astype(jnp.float32), axis=0)
    grad_attended = (
        jnp.einsum("re,de->rd", grad_branch_one, proj_out, preferred_element_type=jnp.float32)
        .astype(jnp.bfloat16)
        .reshape(batch_size, tok_rows, head_count, head_dim)
    )
    delta_rows = jnp.sum(grad_attended.astype(jnp.float32) * attended_full, axis=-1)
    grad_query, grad_keys, grad_values = backward_keys(
        queries, grad_attended, log_total, delta_rows, score_scale, key_all, value_all
    )
    grad_key_own = rings.ctx_scatter_rows(grad_keys.reshape(-1, width_all))
    grad_value_own = rings.ctx_scatter_rows(grad_values.reshape(-1, width_all))
    grad_projected = jnp.concatenate(
        [
            grad_query.reshape(row_count, width_all),
            grad_key_own,
            grad_value_own,
        ],
        axis=1,
    ).astype(jnp.bfloat16)
    grad_in = weight_grad(normed_one_low, grad_projected, input_proj.shape[0])
    grad_normed_one = jnp.einsum(
        "re,de->rd", grad_projected, proj_in, preferred_element_type=jnp.float32
    )
    grad_hidden_norm, grad_gain_one, grad_shift_one = norm_pull_one(grad_normed_one)
    grad_hidden = grad_after + grad_hidden_norm
    grad_types = jnp.einsum("rt,rd->td", onehot, grad_hidden, precision=lax.Precision.HIGHEST)

    small_grads = jnp.concatenate(
        [
            jnp.stack(
                [
                    grad_gain_one,
                    grad_shift_one,
                    grad_out_bias,
                    grad_gain_two,
                    grad_shift_two,
                    grad_down_bias,
                ],
                axis=1,
            ),
            grad_types.T,
            grad_up_bias.reshape(width_all, ff_per_row),
            jnp.broadcast_to(local_square, (width_all, 1)),
        ],
        axis=1,
    )
    small_width = small_grads.shape[1]

    def small_block(b, c0, c1):
        shaped = small_grads.reshape(n_dp, n_ctx, shard_rows, small_width)
        return lax.dynamic_index_in_dim(shaped, b, 1, keepdims=False).reshape(
            n_dp * shard_rows, small_width
        )[:, c0:c1]

    small_own = rings.scatter(small_block, shard_rows, small_width, colors=1)
    loss_value = small_own[0, -1] / (valid_total * width_all)
    owned_gain_one, owned_shift_one, owned_out_bias, owned_gain_two, owned_shift_two = (
        small_own[:, k] for k in range(5)
    )
    owned_down_bias = small_own[:, 5]
    owned_types = small_own[:, 6 : 6 + TYPES].T
    owned_up_bias = small_own[:, 6 + TYPES : 6 + TYPES + ff_per_row].reshape(-1)
    return (
        result.reshape(batch_size, tok_rows, width_all),
        loss_value,
        grad_hidden.reshape(batch_size, tok_rows, width_all),
        owned_types,
        owned_gain_one,
        owned_shift_one,
        grad_in,
        grad_out,
        owned_out_bias,
        owned_gain_two,
        owned_shift_two,
        grad_up,
        owned_up_bias,
        grad_down,
        owned_down_bias,
    )


def solution(mesh):
    subs = dp_subaxes(mesh)

    def step(*args):
        return body(subs, *args)

    return jax.shard_map(
        step,
        mesh=mesh,
        in_specs=(
            P("dp", "ctx", None),
            P("dp", "ctx", None),
            P("dp", "ctx"),
            P("dp", "ctx"),
            P(None, ("dp", "ctx")),
            P(("dp", "ctx")),
            P(("dp", "ctx")),
            P(("dp", "ctx"), None),
            P(("dp", "ctx"), None),
            P(("dp", "ctx")),
            P(("dp", "ctx")),
            P(("dp", "ctx")),
            P(("dp", "ctx"), None),
            P(("dp", "ctx")),
            P(("dp", "ctx"), None),
            P(("dp", "ctx")),
        ),
        out_specs=(
            P("dp", "ctx", None),
            P(),
            P("dp", "ctx", None),
            P(None, ("dp", "ctx")),
            P(("dp", "ctx")),
            P(("dp", "ctx")),
            P(("dp", "ctx"), None),
            P(("dp", "ctx"), None),
            P(("dp", "ctx")),
            P(("dp", "ctx")),
            P(("dp", "ctx")),
            P(("dp", "ctx"), None),
            P(("dp", "ctx")),
            P(("dp", "ctx"), None),
            P(("dp", "ctx")),
        ),
        check_vma=False,
    )
```

```python
import numpy as np

import jax
import jax.numpy as jnp
from jax import lax
from jax.sharding import PartitionSpec as P

HEADS = 16
TYPES = 3


EPSILON = 1e-05


def layer_norm(values, norm_gain, norm_shift):
    centre = values - jnp.mean(values, axis=-1, keepdims=True)
    spread = jnp.mean(centre * centre, axis=-1, keepdims=True)
    return centre * lax.rsqrt(spread + EPSILON) * norm_gain + norm_shift


def gelu_exact(values):
    return jax.nn.gelu(values, approximate=False)


def split_blocks(tensor, head_count):
    batch_size, length, width_all = tensor.shape
    block_size = length
    shaped = tensor.reshape(
        batch_size, length // block_size, block_size, head_count, width_all // head_count
    )
    return jnp.moveaxis(shaped, 1, 0)


def attend_piece(queries, score_scale, carried, arrived):
    key_rows, value_rows = arrived
    head_count = queries.shape[2]
    key_blocks = split_blocks(key_rows, head_count)
    value_blocks = split_blocks(value_rows, head_count)

    def online_step(running, block_pair):
        run_max, run_sum, accumulated = running
        key_block, value_block = block_pair
        scores = (
            jnp.einsum("bqhd,bkhd->bqhk", queries, key_block, preferred_element_type=jnp.float32)
            * score_scale
        )
        new_max = jnp.maximum(run_max, jnp.max(scores, axis=-1))
        factor = jnp.exp(run_max - new_max)
        weights = jnp.exp(scores - new_max[..., None])
        run_sum = run_sum * factor + jnp.sum(weights, axis=-1)
        accumulated = accumulated * factor[..., None] + jnp.einsum(
            "bqhk,bkhd->bqhd",
            weights.astype(jnp.bfloat16),
            value_block,
            preferred_element_type=jnp.float32,
        )
        return ((new_max, run_sum, accumulated), None)

    carried, unused = lax.scan(online_step, carried, (key_blocks, value_blocks))
    return carried


def backward_keys(queries, grad_attended, log_total, delta_rows, score_scale, key_all, value_all):
    head_count = queries.shape[2]
    key_blocks = split_blocks(key_all, head_count)
    value_blocks = split_blocks(value_all, head_count)

    def back_step(grad_query, block_pair):
        key_block, value_block = block_pair
        scores = (
            jnp.einsum("bqhd,bkhd->bqhk", queries, key_block, preferred_element_type=jnp.float32)
            * score_scale
        )
        probs = jnp.exp(scores - log_total[..., None])
        grad_probs = jnp.einsum(
            "bqhd,bkhd->bqhk", grad_attended, value_block, preferred_element_type=jnp.float32
        )
        grad_scores = (probs * (grad_probs - delta_rows[..., None])).astype(jnp.bfloat16)
        grad_query = (
            grad_query
            + jnp.einsum(
                "bqhk,bkhd->bqhd", grad_scores, key_block, preferred_element_type=jnp.float32
            )
            * score_scale
        )
        grad_key = (
            jnp.einsum("bqhk,bqhd->bkhd", grad_scores, queries, preferred_element_type=jnp.float32)
            * score_scale
        )
        grad_value = jnp.einsum(
            "bqhk,bqhd->bkhd",
            probs.astype(jnp.bfloat16),
            grad_attended,
            preferred_element_type=jnp.float32,
        )
        return (grad_query, (grad_key, grad_value))

    initial = jnp.zeros(queries.shape, jnp.float32)
    grad_query, (key_parts, value_parts) = lax.scan(back_step, initial, (key_blocks, value_blocks))
    batch_size, length = (key_all.shape[0], key_all.shape[1])
    grad_keys = jnp.moveaxis(key_parts, 0, 1).reshape(batch_size, length, -1)
    grad_values = jnp.moveaxis(value_parts, 0, 1).reshape(batch_size, length, -1)
    return (grad_query, grad_keys, grad_values)


def dp_subaxes(mesh):
    devs = np.asarray(mesh.devices)
    n_dp = devs.shape[0]
    single = ((n_dp, 1),)
    try:
        coords = [tuple(int(v) for v in d.coords) for d in devs[:, 0]]
    except Exception:
        return single
    rank = len(coords[0])
    subs = []
    stride = 1
    while stride < n_dp:
        diff = [k for k in range(rank) if coords[stride][k] != coords[0][k]]
        if len(diff) != 1 or n_dp % stride:
            return single
        axis = diff[0]
        size = 1
        while size * stride < n_dp:
            here = coords[size * stride]
            same_rest = all(here[k] == coords[0][k] for k in range(rank) if k != axis)
            if here[axis] == coords[0][axis] or not same_rest:
                break
            size += 1
        if n_dp % (stride * size):
            return single
        subs.append((size, stride))
        stride *= size
    if stride != n_dp:
        return single
    return tuple(subs)


def _ring_perm(n_axis, size, stride):
    pairs = []
    for i in range(n_axis):
        digit = (i // stride) % size
        pairs.append((i, i + (((digit + 1) % size) - digit) * stride))
    return pairs


def _digit(me, size, stride):
    return (me // stride) % size


def _ring_rs(block_of, n, me, axis, perm):
    if n == 1:
        return block_of(0)
    acc = block_of((me + n - 1) % n)
    for step in range(n - 1):
        acc = lax.ppermute(acc, axis, perm) + block_of((me + 2 * n - 2 - step) % n)
    return acc


def _ring_ag(piece, n, me, axis, perm, dim):
    if n == 1:
        return jnp.expand_dims(piece, dim)
    out = jnp.zeros(piece.shape[:dim] + (n,) + piece.shape[dim:], piece.dtype)
    out = lax.dynamic_update_index_in_dim(out, piece, me, dim)
    cur = piece
    for step in range(1, n):
        cur = lax.ppermute(cur, axis, perm)
        out = lax.dynamic_update_index_in_dim(out, cur, (me + n - step) % n, dim)
    return out


class Rings:
    def __init__(self, subs, n_dp, n_ctx):
        self.subs = subs
        self.n_dp = n_dp
        self.n_ctx = n_ctx
        self.dp_perms = [_ring_perm(n_dp, size, stride) for size, stride in subs]
        self.ctx_perm = _ring_perm(n_ctx, n_ctx, 1)
        order = sorted(range(len(subs)), key=lambda k: subs[k][0])
        swapped = list(order)
        if len(swapped) >= 2:
            swapped[0], swapped[1] = swapped[1], swapped[0]
        self.rs_orders = (order, swapped)
        self.me_dp = lax.axis_index("dp")
        self.me_ctx = lax.axis_index("ctx")

    def _col_parts(self, width, colors):
        if colors > 1 and width % (128 * colors) == 0:
            step = width // colors
            return [(k * step, (k + 1) * step) for k in range(colors)]
        return [(0, width)]

    def _gather_rel(self, piece, order):
        coll = piece[None]
        rel_strides = {}
        span = 1
        for k in order:
            size, stride = self.subs[k]
            blocks = [coll]
            cur = coll
            for step in range(1, size):
                cur = lax.ppermute(cur, "dp", self.dp_perms[k])
                blocks.append(cur)
            coll = jnp.concatenate(blocks, axis=0) if size > 1 else coll
            rel_strides[k] = span
            span *= size
        if self.n_ctx > 1:
            blocks = [coll]
            cur = coll
            for step in range(1, self.n_ctx):
                cur = lax.ppermute(cur, "ctx", self.ctx_perm)
                blocks.append(cur)
            coll = jnp.concatenate(blocks, axis=0)
        ctx_stride = span
        absolute = jnp.arange(self.n_dp * self.n_ctx, dtype=jnp.int32)
        a_dp = absolute // self.n_ctx
        a_ctx = absolute % self.n_ctx
        index = ((self.me_ctx - a_ctx) % self.n_ctx) * ctx_stride
        for k, (size, stride) in enumerate(self.subs):
            rel = (_digit(self.me_dp, size, stride) - _digit(a_dp, size, stride)) % size
            index = index + rel * rel_strides[k]
        return coll, index

    def gather_group(self, shards, colors=2):
        flat = []
        sizes = []
        for shard in shards:
            count = shard.size
            lines = -(-count // 128)
            line = shard.reshape(count)
            if lines * 128 != count:
                line = jnp.pad(line, (0, lines * 128 - count))
            flat.append(line.reshape(lines, 128))
            sizes.append(lines)
        buf = jnp.concatenate(flat, axis=0)
        total = buf.shape[0]
        cuts = [0, total]
        if colors > 1 and total >= 32 * colors:
            cuts = [0] + [(total * k // colors) // 16 * 16 for k in range(1, colors)] + [total]
        outs = []
        for color in range(len(cuts) - 1):
            part = buf[cuts[color] : cuts[color + 1]]
            coll, index = self._gather_rel(part, list(reversed(self.rs_orders[color % 2])))
            outs.append(jnp.take(coll, index, axis=0))
        full = outs[0] if len(outs) == 1 else jnp.concatenate(outs, axis=1)
        n_all = self.n_dp * self.n_ctx
        results = []
        at = 0
        for shard, lines in zip(shards, sizes):
            rows, width = shard.shape
            part = full[:, at : at + lines].reshape(n_all, lines * 128)
            if lines * 128 != rows * width:
                part = part[:, : rows * width]
            results.append(part.reshape(n_all * rows, width))
            at += lines
        return results

    def scatter_dp(self, acc, rows, width, colors=2, send_dtype=jnp.bfloat16):
        pieces = []
        for color, (c0, c1) in enumerate(self._col_parts(width, colors)):
            shape = tuple(size for size, _ in reversed(self.subs)) + (rows, c1 - c0)
            cur_acc = acc[:, c0:c1].reshape(shape)
            left = list(range(len(self.subs)))
            for k in self.rs_orders[color % 2]:
                size, stride = self.subs[k]
                pos = sum(1 for g in left if g > k)
                held = cur_acc
                cur_acc = _ring_rs_cast(
                    lambda b, held=held, pos=pos: lax.dynamic_index_in_dim(
                        held, b, pos, keepdims=False
                    ),
                    size,
                    _digit(self.me_dp, size, stride),
                    "dp",
                    self.dp_perms[k],
                    send_dtype,
                )
                left.remove(k)
            pieces.append(cur_acc)
        if len(pieces) == 1:
            return pieces[0]
        return jnp.concatenate(pieces, axis=1)

    def scatter(self, block_of, rows, width, colors=2, send_dtype=jnp.bfloat16):
        acc = _ring_rs(block_of, self.n_ctx, self.me_ctx, "ctx", self.ctx_perm)
        return self.scatter_dp(acc, rows, width, colors, send_dtype)

    def ctx_gather_rows(self, piece):
        out = _ring_ag(piece, self.n_ctx, self.me_ctx, "ctx", self.ctx_perm, 0)
        return out.reshape((-1,) + piece.shape[1:])

    def ctx_scatter_rows(self, full):
        shaped = full.reshape((self.n_ctx, -1) + full.shape[1:])
        return _ring_rs(
            lambda b: lax.dynamic_index_in_dim(shaped, b, 0, keepdims=False),
            self.n_ctx,
            self.me_ctx,
            "ctx",
            self.ctx_perm,
        )


def _ring_rs_cast(block_of, n, me, axis, perm, send_dtype):
    if n == 1:
        return block_of(0)
    acc = block_of((me + n - 1) % n)
    for step in range(n - 1):
        moved = lax.ppermute(acc.astype(send_dtype), axis, perm).astype(acc.dtype)
        acc = moved + block_of((me + 2 * n - 2 - step) % n)
    return acc


def _ctx_block_cols(values, n_dp, n_ctx, rows, b):
    tok = values.shape[0]
    shaped = values.reshape(tok, n_dp, n_ctx, rows)
    return lax.dynamic_index_in_dim(shaped, b, 2, keepdims=False).reshape(tok, n_dp * rows)


def body(
    subs,
    inputs,
    teacher,
    valid_mask,
    token_types,
    type_table,
    first_gain,
    first_shift,
    input_proj,
    output_proj,
    output_bias,
    second_gain,
    second_shift,
    up_proj,
    up_bias,
    down_proj,
    down_bias,
):
    batch_size, tok_rows, width_all = inputs.shape
    row_count = batch_size * tok_rows
    head_count = HEADS
    head_dim = width_all // head_count
    score_scale = head_dim ** (-0.5)
    n_dp = lax.axis_size("dp")
    n_ctx = lax.axis_size("ctx")
    rings = Rings(subs, n_dp, n_ctx)
    shard_rows = first_gain.shape[0]
    ff_all = up_proj.shape[1]
    ff_per_row = ff_all // width_all
    mask_rows = valid_mask.reshape(row_count).astype(jnp.float32)

    count = jnp.sum(valid_mask)
    first_row = (jnp.arange(shard_rows) == 0)[:, None]
    count_cols = jnp.where(
        first_row,
        jnp.stack([count // 16, count % 16]).astype(jnp.bfloat16)[None, :],
        jnp.zeros((1, 2), jnp.bfloat16),
    )
    small = jnp.concatenate(
        [
            type_table.T,
            jnp.stack(
                [first_gain, first_shift, output_bias, second_gain, second_shift, down_bias],
                axis=1,
            ),
            up_bias.reshape(shard_rows, ff_per_row),
            count_cols,
            jnp.zeros((shard_rows, 1), jnp.bfloat16),
        ],
        axis=1,
    )
    small_all, proj_in = rings.gather_group([small, input_proj])
    small_all = small_all.astype(jnp.float32)
    table_full = small_all[:, 0:TYPES].T
    gain_one, shift_one, bias_out, gain_two, shift_two, bias_down = (
        small_all[:, TYPES + k] for k in range(6)
    )
    bias_up = small_all[:, TYPES + 6 : TYPES + 6 + ff_per_row].reshape(ff_all)
    count_at = TYPES + 6 + ff_per_row
    valid_total = jnp.sum(small_all[:, count_at]) * 16.0 + jnp.sum(small_all[:, count_at + 1])

    proj_out, proj_up, proj_down = rings.gather_group([output_proj, up_proj, down_proj])

    onehot = (
        token_types.reshape(row_count)[:, None] == jnp.arange(TYPES, dtype=jnp.int32)[None, :]
    ).astype(jnp.float32)
    hidden = inputs.reshape(row_count, width_all).astype(jnp.float32) + jnp.dot(
        onehot, table_full, precision=lax.Precision.HIGHEST
    )
    normed_one, norm_pull_one = jax.vjp(layer_norm, hidden, gain_one, shift_one)
    normed_one_low = normed_one.astype(jnp.bfloat16)
    projected = jnp.dot(normed_one_low, proj_in, preferred_element_type=jnp.float32).astype(
        jnp.bfloat16
    )
    queries = projected[:, :width_all].reshape(batch_size, tok_rows, head_count, head_dim)
    key_rows = projected[:, width_all : 2 * width_all]
    value_rows = projected[:, 2 * width_all :]
    key_all = rings.ctx_gather_rows(key_rows).reshape(batch_size, -1, width_all)
    value_all = rings.ctx_gather_rows(value_rows).reshape(batch_size, -1, width_all)
    start_state = (
        jnp.full((batch_size, tok_rows, head_count), -1e30, jnp.float32),
        jnp.zeros((batch_size, tok_rows, head_count), jnp.float32),
        jnp.zeros((batch_size, tok_rows, head_count, head_dim), jnp.float32),
    )
    running = attend_piece(queries, score_scale, start_state, (key_all, value_all))
    run_max, run_sum, accumulated = running
    attended_full = accumulated / run_sum[..., None]
    log_total = run_max + jnp.log(run_sum)
    attended_low = attended_full.reshape(row_count, width_all).astype(jnp.bfloat16)
    after_attn = (
        hidden
        + jnp.dot(attended_low, proj_out, preferred_element_type=jnp.float32)
        + bias_out
    )
    normed_two, norm_pull_two = jax.vjp(layer_norm, after_attn, gain_two, shift_two)
    normed_two_low = normed_two.astype(jnp.bfloat16)
    pre_act = jnp.dot(normed_two_low, proj_up, preferred_element_type=jnp.float32) + bias_up
    activ_full, gelu_pull = jax.vjp(gelu_exact, pre_act)
    activ_low = activ_full.astype(jnp.bfloat16)
    result = (
        after_attn
        + jnp.dot(activ_low, proj_down, preferred_element_type=jnp.float32)
        + bias_down
    )
    error_rows = result - teacher.reshape(row_count, width_all).astype(jnp.float32)
    local_square = jnp.sum(mask_rows[:, None] * error_rows * error_rows)
    rows_all = row_count * n_dp * n_ctx
    grad_act = 2.0 * rows_all / valid_total * mask_rows[:, None] * error_rows

    def weight_grad(left, right, rows):
        tok = left.shape[0]
        ctx_major = (
            left.reshape(tok, n_dp, n_ctx, rows)
            .transpose(0, 2, 1, 3)
            .reshape(tok, n_ctx * n_dp * rows)
        )
        full = jnp.einsum(
            "rd,re->de", ctx_major, right, preferred_element_type=jnp.float32
        ).reshape(n_ctx, n_dp * rows, right.shape[1])
        acc = _ring_rs(
            lambda b: lax.dynamic_index_in_dim(full, b, 0, keepdims=False),
            n_ctx,
            rings.me_ctx,
            "ctx",
            rings.ctx_perm,
        )
        return rings.scatter_dp(acc, rows, right.shape[1])

    grad_branch_two = grad_act.astype(jnp.bfloat16)
    grad_down = weight_grad(activ_low, grad_branch_two, down_proj.shape[0])
    grad_down_bias = jnp.sum(grad_branch_two.astype(jnp.float32), axis=0)
    grad_activ = jnp.einsum(
        "rd,fd->rf", grad_branch_two, proj_down, preferred_element_type=jnp.float32
    )
    grad_pre = gelu_pull(grad_activ)[0].astype(jnp.bfloat16)
    grad_up = weight_grad(normed_two_low, grad_pre, up_proj.shape[0])
    grad_up_bias = jnp.sum(grad_pre.astype(jnp.float32), axis=0)
    grad_normed_two = jnp.einsum("rf,df->rd", grad_pre, proj_up, preferred_element_type=jnp.float32)
    grad_after_norm, grad_gain_two, grad_shift_two = norm_pull_two(grad_normed_two)
    grad_after = grad_act + grad_after_norm
    grad_branch_one = grad_after.astype(jnp.bfloat16)
    grad_out = weight_grad(attended_low, grad_branch_one, output_proj.shape[0])
    grad_out_bias = jnp.sum(grad_branch_one.astype(jnp.float32), axis=0)
    grad_attended = (
        jnp.einsum("re,de->rd", grad_branch_one, proj_out, preferred_element_type=jnp.float32)
        .astype(jnp.bfloat16)
        .reshape(batch_size, tok_rows, head_count, head_dim)
    )
    delta_rows = jnp.sum(grad_attended.astype(jnp.float32) * attended_full, axis=-1)
    grad_query, grad_keys, grad_values = backward_keys(
        queries, grad_attended, log_total, delta_rows, score_scale, key_all, value_all
    )
    grad_key_own = rings.ctx_scatter_rows(grad_keys.reshape(-1, width_all))
    grad_value_own = rings.ctx_scatter_rows(grad_values.reshape(-1, width_all))
    grad_projected = jnp.concatenate(
        [
            grad_query.reshape(row_count, width_all),
            grad_key_own,
            grad_value_own,
        ],
        axis=1,
    ).astype(jnp.bfloat16)
    grad_in = weight_grad(normed_one_low, grad_projected, input_proj.shape[0])
    grad_normed_one = jnp.einsum(
        "re,de->rd", grad_projected, proj_in, preferred_element_type=jnp.float32
    )
    grad_hidden_norm, grad_gain_one, grad_shift_one = norm_pull_one(grad_normed_one)
    grad_hidden = grad_after + grad_hidden_norm
    grad_types = jnp.einsum("rt,rd->td", onehot, grad_hidden, precision=lax.Precision.HIGHEST)

    small_grads = jnp.concatenate(
        [
            jnp.stack(
                [
                    grad_gain_one,
                    grad_shift_one,
                    grad_out_bias,
                    grad_gain_two,
                    grad_shift_two,
                    grad_down_bias,
                ],
                axis=1,
            ),
            grad_types.T,
            grad_up_bias.reshape(width_all, ff_per_row),
            jnp.broadcast_to(local_square, (width_all, 1)),
        ],
        axis=1,
    )
    small_width = small_grads.shape[1]

    def small_block(b):
        shaped = small_grads.reshape(n_dp, n_ctx, shard_rows, small_width)
        return lax.dynamic_index_in_dim(shaped, b, 1, keepdims=False).reshape(
            n_dp * shard_rows, small_width
        )

    small_own = rings.scatter(
        small_block, shard_rows, small_width, colors=1, send_dtype=jnp.float32
    )
    loss_value = small_own[0, -1] / (valid_total * width_all)
    owned_gain_one, owned_shift_one, owned_out_bias, owned_gain_two, owned_shift_two = (
        small_own[:, k] for k in range(5)
    )
    owned_down_bias = small_own[:, 5]
    owned_types = small_own[:, 6 : 6 + TYPES].T
    owned_up_bias = small_own[:, 6 + TYPES : 6 + TYPES + ff_per_row].reshape(-1)
    return (
        result.reshape(batch_size, tok_rows, width_all),
        loss_value,
        grad_hidden.reshape(batch_size, tok_rows, width_all),
        owned_types,
        owned_gain_one,
        owned_shift_one,
        grad_in,
        grad_out,
        owned_out_bias,
        owned_gain_two,
        owned_shift_two,
        grad_up,
        owned_up_bias,
        grad_down,
        owned_down_bias,
    )


def solution(mesh):
    subs = dp_subaxes(mesh)

    def step(*args):
        return body(subs, *args)

    return jax.shard_map(
        step,
        mesh=mesh,
        in_specs=(
            P("dp", "ctx", None),
            P("dp", "ctx", None),
            P("dp", "ctx"),
            P("dp", "ctx"),
            P(None, ("dp", "ctx")),
            P(("dp", "ctx")),
            P(("dp", "ctx")),
            P(("dp", "ctx"), None),
            P(("dp", "ctx"), None),
            P(("dp", "ctx")),
            P(("dp", "ctx")),
            P(("dp", "ctx")),
            P(("dp", "ctx"), None),
            P(("dp", "ctx")),
            P(("dp", "ctx"), None),
            P(("dp", "ctx")),
        ),
        out_specs=(
            P("dp", "ctx", None),
            P(),
            P("dp", "ctx", None),
            P(None, ("dp", "ctx")),
            P(("dp", "ctx")),
            P(("dp", "ctx")),
            P(("dp", "ctx"), None),
            P(("dp", "ctx"), None),
            P(("dp", "ctx")),
            P(("dp", "ctx")),
            P(("dp", "ctx")),
            P(("dp", "ctx"), None),
            P(("dp", "ctx")),
            P(("dp", "ctx"), None),
            P(("dp", "ctx")),
        ),
        check_vma=False,
    )
```

```python
import numpy as np

import jax
import jax.numpy as jnp
from jax import lax
from jax.sharding import PartitionSpec as P

HEADS = 16
TYPES = 3


EPSILON = 1e-05


def layer_norm(values, norm_gain, norm_shift):
    centre = values - jnp.mean(values, axis=-1, keepdims=True)
    spread = jnp.mean(centre * centre, axis=-1, keepdims=True)
    return centre * lax.rsqrt(spread + EPSILON) * norm_gain + norm_shift


def gelu_exact(values):
    return jax.nn.gelu(values, approximate=False)


def split_blocks(tensor, head_count):
    batch_size, length, width_all = tensor.shape
    block_size = length
    shaped = tensor.reshape(
        batch_size, length // block_size, block_size, head_count, width_all // head_count
    )
    return jnp.moveaxis(shaped, 1, 0)


def attend_piece(queries, score_scale, carried, arrived):
    key_rows, value_rows = arrived
    head_count = queries.shape[2]
    key_blocks = split_blocks(key_rows, head_count)
    value_blocks = split_blocks(value_rows, head_count)

    def online_step(running, block_pair):
        run_max, run_sum, accumulated = running
        key_block, value_block = block_pair
        scores = (
            jnp.einsum("bqhd,bkhd->bqhk", queries, key_block, preferred_element_type=jnp.float32)
            * score_scale
        )
        new_max = jnp.maximum(run_max, jnp.max(scores, axis=-1))
        factor = jnp.exp(run_max - new_max)
        weights = jnp.exp(scores - new_max[..., None])
        run_sum = run_sum * factor + jnp.sum(weights, axis=-1)
        accumulated = accumulated * factor[..., None] + jnp.einsum(
            "bqhk,bkhd->bqhd",
            weights.astype(jnp.bfloat16),
            value_block,
            preferred_element_type=jnp.float32,
        )
        return ((new_max, run_sum, accumulated), None)

    carried, unused = lax.scan(online_step, carried, (key_blocks, value_blocks))
    return carried


def backward_keys(queries, grad_attended, log_total, delta_rows, score_scale, key_all, value_all):
    head_count = queries.shape[2]
    key_blocks = split_blocks(key_all, head_count)
    value_blocks = split_blocks(value_all, head_count)

    def back_step(grad_query, block_pair):
        key_block, value_block = block_pair
        scores = (
            jnp.einsum("bqhd,bkhd->bqhk", queries, key_block, preferred_element_type=jnp.float32)
            * score_scale
        )
        probs = jnp.exp(scores - log_total[..., None])
        grad_probs = jnp.einsum(
            "bqhd,bkhd->bqhk", grad_attended, value_block, preferred_element_type=jnp.float32
        )
        grad_scores = (probs * (grad_probs - delta_rows[..., None])).astype(jnp.bfloat16)
        grad_query = (
            grad_query
            + jnp.einsum(
                "bqhk,bkhd->bqhd", grad_scores, key_block, preferred_element_type=jnp.float32
            )
            * score_scale
        )
        grad_key = (
            jnp.einsum("bqhk,bqhd->bkhd", grad_scores, queries, preferred_element_type=jnp.float32)
            * score_scale
        )
        grad_value = jnp.einsum(
            "bqhk,bqhd->bkhd",
            probs.astype(jnp.bfloat16),
            grad_attended,
            preferred_element_type=jnp.float32,
        )
        return (grad_query, (grad_key, grad_value))

    initial = jnp.zeros(queries.shape, jnp.float32)
    grad_query, (key_parts, value_parts) = lax.scan(back_step, initial, (key_blocks, value_blocks))
    batch_size, length = (key_all.shape[0], key_all.shape[1])
    grad_keys = jnp.moveaxis(key_parts, 0, 1).reshape(batch_size, length, -1)
    grad_values = jnp.moveaxis(value_parts, 0, 1).reshape(batch_size, length, -1)
    return (grad_query, grad_keys, grad_values)


def dp_subaxes(mesh):
    devs = np.asarray(mesh.devices)
    n_dp = devs.shape[0]
    single = ((n_dp, 1),)
    try:
        coords = [tuple(int(v) for v in d.coords) for d in devs[:, 0]]
    except Exception:
        return single
    rank = len(coords[0])
    subs = []
    stride = 1
    while stride < n_dp:
        diff = [k for k in range(rank) if coords[stride][k] != coords[0][k]]
        if len(diff) != 1 or n_dp % stride:
            return single
        axis = diff[0]
        size = 1
        while size * stride < n_dp:
            here = coords[size * stride]
            same_rest = all(here[k] == coords[0][k] for k in range(rank) if k != axis)
            if here[axis] == coords[0][axis] or not same_rest:
                break
            size += 1
        if n_dp % (stride * size):
            return single
        subs.append((size, stride))
        stride *= size
    if stride != n_dp:
        return single
    return tuple(subs)


def _ring_perm(n_axis, size, stride):
    pairs = []
    for i in range(n_axis):
        digit = (i // stride) % size
        pairs.append((i, i + (((digit + 1) % size) - digit) * stride))
    return pairs


def _digit(me, size, stride):
    return (me // stride) % size


def _ring_rs(block_of, n, me, axis, perm):
    if n == 1:
        return block_of(0)
    acc = block_of((me + n - 1) % n)
    for step in range(n - 1):
        acc = lax.ppermute(acc, axis, perm) + block_of((me + 2 * n - 2 - step) % n)
    return acc


def _ring_ag(piece, n, me, axis, perm, dim):
    if n == 1:
        return jnp.expand_dims(piece, dim)
    out = jnp.zeros(piece.shape[:dim] + (n,) + piece.shape[dim:], piece.dtype)
    out = lax.dynamic_update_index_in_dim(out, piece, me, dim)
    cur = piece
    for step in range(1, n):
        cur = lax.ppermute(cur, axis, perm)
        out = lax.dynamic_update_index_in_dim(out, cur, (me + n - step) % n, dim)
    return out


class Rings:
    def __init__(self, subs, n_dp, n_ctx):
        self.subs = subs
        self.n_dp = n_dp
        self.n_ctx = n_ctx
        self.dp_perms = [_ring_perm(n_dp, size, stride) for size, stride in subs]
        self.ctx_perm = _ring_perm(n_ctx, n_ctx, 1)
        order = sorted(range(len(subs)), key=lambda k: subs[k][0])
        swapped = list(order)
        if len(swapped) >= 2:
            swapped[0], swapped[1] = swapped[1], swapped[0]
        self.rs_orders = (order, swapped)
        self.me_dp = lax.axis_index("dp")
        self.me_ctx = lax.axis_index("ctx")

    def _col_parts(self, width, colors):
        if colors > 1 and width % (128 * colors) == 0:
            step = width // colors
            return [(k * step, (k + 1) * step) for k in range(colors)]
        return [(0, width)]

    def _place(self, pieces, me, dim):
        n = len(pieces)
        if n == 1:
            return jnp.expand_dims(pieces[0], dim)
        if n == 2:
            first = me == 0
            ordered = [jnp.where(first, pieces[0], pieces[1]), jnp.where(first, pieces[1], pieces[0])]
        else:
            ordered = [lax.select_n((me + n - a) % n, *pieces) for a in range(n)]
        return jnp.stack(ordered, axis=dim)

    def _ring_pieces(self, piece, n, axis, perm):
        pieces = [piece]
        cur = piece
        for step in range(1, n):
            cur = lax.ppermute(cur, axis, perm)
            pieces.append(cur)
        return pieces

    def gather(self, shard, colors=2):
        rows, width = shard.shape
        if colors < 2 or rows % (8 * colors):
            colors = 1
        sub = rows // colors
        per_color = []
        for color in range(colors):
            part = shard[color * sub : (color + 1) * sub]
            done = []
            for k in reversed(self.rs_orders[color % 2]):
                size, stride = self.subs[k]
                pos = sum(1 for g in done if g > k)
                pieces = self._ring_pieces(part, size, "dp", self.dp_perms[k])
                part = self._place(pieces, _digit(self.me_dp, size, stride), pos)
                done.append(k)
            part = part.reshape((self.n_dp, sub, width))
            per_color.append(self._ring_pieces(part, self.n_ctx, "ctx", self.ctx_perm))
        n = self.n_ctx
        me = self.me_ctx
        ordered = []
        for a in range(n):
            for color in range(colors):
                pieces = per_color[color]
                if n == 1:
                    ordered.append(pieces[0])
                elif n == 2:
                    ordered.append(jnp.where(me == a, pieces[0], pieces[1]))
                else:
                    ordered.append(lax.select_n((me + n - a) % n, *pieces))
        out = jnp.stack(ordered, axis=1)
        return out.reshape((self.n_dp * n * rows, width))

    def scatter_dp(self, acc, rows, width, colors=2, send_dtype=jnp.bfloat16):
        pieces = []
        for color, (c0, c1) in enumerate(self._col_parts(width, colors)):
            shape = tuple(size for size, _ in reversed(self.subs)) + (rows, c1 - c0)
            cur_acc = acc[:, c0:c1].reshape(shape)
            left = list(range(len(self.subs)))
            for k in self.rs_orders[color % 2]:
                size, stride = self.subs[k]
                pos = sum(1 for g in left if g > k)
                held = cur_acc
                cur_acc = _ring_rs_cast(
                    lambda b, held=held, pos=pos: lax.dynamic_index_in_dim(
                        held, b, pos, keepdims=False
                    ),
                    size,
                    _digit(self.me_dp, size, stride),
                    "dp",
                    self.dp_perms[k],
                    send_dtype,
                )
                left.remove(k)
            pieces.append(cur_acc)
        if len(pieces) == 1:
            return pieces[0]
        return jnp.concatenate(pieces, axis=1)

    def scatter(self, block_of, rows, width, colors=2, send_dtype=jnp.bfloat16):
        acc = _ring_rs(block_of, self.n_ctx, self.me_ctx, "ctx", self.ctx_perm)
        return self.scatter_dp(acc, rows, width, colors, send_dtype)

    def ctx_gather_rows(self, piece):
        pieces = self._ring_pieces(piece, self.n_ctx, "ctx", self.ctx_perm)
        return jnp.concatenate(pieces, axis=0)

    def ctx_scatter_rows(self, full):
        n = self.n_ctx
        shaped = full.reshape((n, -1) + full.shape[1:])
        if n == 1:
            return shaped[0]
        acc = shaped[1]
        for step in range(n - 1):
            acc = lax.ppermute(acc, "ctx", self.ctx_perm) + shaped[(step + 2) % n]
        return acc


def _ring_rs_cast(block_of, n, me, axis, perm, send_dtype):
    if n == 1:
        return block_of(0)
    acc = block_of((me + n - 1) % n)
    for step in range(n - 1):
        moved = lax.ppermute(acc.astype(send_dtype), axis, perm).astype(acc.dtype)
        acc = moved + block_of((me + 2 * n - 2 - step) % n)
    return acc


def _ctx_block_cols(values, n_dp, n_ctx, rows, b):
    tok = values.shape[0]
    shaped = values.reshape(tok, n_dp, n_ctx, rows)
    return lax.dynamic_index_in_dim(shaped, b, 2, keepdims=False).reshape(tok, n_dp * rows)


def body(
    subs,
    inputs,
    teacher,
    valid_mask,
    token_types,
    type_table,
    first_gain,
    first_shift,
    input_proj,
    output_proj,
    output_bias,
    second_gain,
    second_shift,
    up_proj,
    up_bias,
    down_proj,
    down_bias,
):
    batch_size, tok_rows, width_all = inputs.shape
    row_count = batch_size * tok_rows
    head_count = HEADS
    head_dim = width_all // head_count
    score_scale = head_dim ** (-0.5)
    n_dp = lax.axis_size("dp")
    n_ctx = lax.axis_size("ctx")
    rings = Rings(subs, n_dp, n_ctx)
    shard_rows = first_gain.shape[0]
    ff_all = up_proj.shape[1]
    ff_per_row = ff_all // width_all
    mask_rows = valid_mask.reshape(row_count).astype(jnp.float32)

    count = jnp.sum(valid_mask)
    first_row = (jnp.arange(shard_rows) == 0)[:, None]
    count_cols = jnp.where(
        first_row,
        jnp.stack([count // 16, count % 16]).astype(jnp.bfloat16)[None, :],
        jnp.zeros((1, 2), jnp.bfloat16),
    )
    small = jnp.concatenate(
        [
            type_table.T,
            jnp.stack(
                [first_gain, first_shift, output_bias, second_gain, second_shift, down_bias],
                axis=1,
            ),
            up_bias.reshape(shard_rows, ff_per_row),
            count_cols,
            jnp.zeros((shard_rows, 1), jnp.bfloat16),
        ],
        axis=1,
    )
    small_all = rings.gather(small, colors=1)
    proj_in = rings.gather(input_proj)
    small_all = small_all.astype(jnp.float32)
    table_full = small_all[:, 0:TYPES].T
    gain_one, shift_one, bias_out, gain_two, shift_two, bias_down = (
        small_all[:, TYPES + k] for k in range(6)
    )
    bias_up = small_all[:, TYPES + 6 : TYPES + 6 + ff_per_row].reshape(ff_all)
    count_at = TYPES + 6 + ff_per_row
    valid_total = jnp.sum(small_all[:, count_at]) * 16.0 + jnp.sum(small_all[:, count_at + 1])

    proj_out = rings.gather(output_proj)
    proj_up = rings.gather(up_proj)
    proj_down = rings.gather(down_proj)

    onehot = (
        token_types.reshape(row_count)[:, None] == jnp.arange(TYPES, dtype=jnp.int32)[None, :]
    ).astype(jnp.float32)
    hidden = inputs.reshape(row_count, width_all).astype(jnp.float32) + jnp.dot(
        onehot, table_full, precision=lax.Precision.HIGHEST
    )
    normed_one, norm_pull_one = jax.vjp(layer_norm, hidden, gain_one, shift_one)
    normed_one_low = normed_one.astype(jnp.bfloat16)
    projected = jnp.dot(normed_one_low, proj_in, preferred_element_type=jnp.float32).astype(
        jnp.bfloat16
    )
    queries = projected[:, :width_all].reshape(batch_size, tok_rows, head_count, head_dim)
    key_rows = projected[:, width_all : 2 * width_all]
    value_rows = projected[:, 2 * width_all :]
    key_all = rings.ctx_gather_rows(key_rows).reshape(batch_size, -1, width_all)
    value_all = rings.ctx_gather_rows(value_rows).reshape(batch_size, -1, width_all)
    start_state = (
        jnp.full((batch_size, tok_rows, head_count), -1e30, jnp.float32),
        jnp.zeros((batch_size, tok_rows, head_count), jnp.float32),
        jnp.zeros((batch_size, tok_rows, head_count, head_dim), jnp.float32),
    )
    running = attend_piece(queries, score_scale, start_state, (key_all, value_all))
    run_max, run_sum, accumulated = running
    attended_full = accumulated / run_sum[..., None]
    log_total = run_max + jnp.log(run_sum)
    attended_low = attended_full.reshape(row_count, width_all).astype(jnp.bfloat16)
    after_attn = (
        hidden
        + jnp.dot(attended_low, proj_out, preferred_element_type=jnp.float32)
        + bias_out
    )
    normed_two, norm_pull_two = jax.vjp(layer_norm, after_attn, gain_two, shift_two)
    normed_two_low = normed_two.astype(jnp.bfloat16)
    pre_act = jnp.dot(normed_two_low, proj_up, preferred_element_type=jnp.float32) + bias_up
    activ_full, gelu_pull = jax.vjp(gelu_exact, pre_act)
    activ_low = activ_full.astype(jnp.bfloat16)
    result = (
        after_attn
        + jnp.dot(activ_low, proj_down, preferred_element_type=jnp.float32)
        + bias_down
    )
    error_rows = result - teacher.reshape(row_count, width_all).astype(jnp.float32)
    local_square = jnp.sum(mask_rows[:, None] * error_rows * error_rows)
    rows_all = row_count * n_dp * n_ctx
    grad_act = 2.0 * rows_all / valid_total * mask_rows[:, None] * error_rows

    def weight_grad(left, right, rows):
        tok = left.shape[0]
        by_ctx = left.reshape(tok, n_dp, n_ctx, rows)
        blocks = [
            jnp.einsum(
                "tdr,te->dre", by_ctx[:, :, b, :], right, preferred_element_type=jnp.float32
            ).reshape(n_dp * rows, right.shape[1])
            for b in range(n_ctx)
        ]

        def block_of(b):
            if n_ctx == 2:
                return jnp.where(b == 0, blocks[0], blocks[1])
            return lax.select_n(b, *blocks)

        acc = _ring_rs(block_of, n_ctx, rings.me_ctx, "ctx", rings.ctx_perm)
        return rings.scatter_dp(acc, rows, right.shape[1])

    grad_branch_two = grad_act.astype(jnp.bfloat16)
    grad_down = weight_grad(activ_low, grad_branch_two, down_proj.shape[0])
    grad_down_bias = jnp.sum(grad_branch_two.astype(jnp.float32), axis=0)
    grad_activ = jnp.einsum(
        "rd,fd->rf", grad_branch_two, proj_down, preferred_element_type=jnp.float32
    )
    grad_pre = gelu_pull(grad_activ)[0].astype(jnp.bfloat16)
    grad_up = weight_grad(normed_two_low, grad_pre, up_proj.shape[0])
    grad_up_bias = jnp.sum(grad_pre.astype(jnp.float32), axis=0)
    grad_normed_two = jnp.einsum("rf,df->rd", grad_pre, proj_up, preferred_element_type=jnp.float32)
    grad_after_norm, grad_gain_two, grad_shift_two = norm_pull_two(grad_normed_two)
    grad_after = grad_act + grad_after_norm
    grad_branch_one = grad_after.astype(jnp.bfloat16)
    grad_out = weight_grad(attended_low, grad_branch_one, output_proj.shape[0])
    grad_out_bias = jnp.sum(grad_branch_one.astype(jnp.float32), axis=0)
    grad_attended = (
        jnp.einsum("re,de->rd", grad_branch_one, proj_out, preferred_element_type=jnp.float32)
        .astype(jnp.bfloat16)
        .reshape(batch_size, tok_rows, head_count, head_dim)
    )
    delta_rows = jnp.sum(grad_attended.astype(jnp.float32) * attended_full, axis=-1)
    grad_query, grad_keys, grad_values = backward_keys(
        queries, grad_attended, log_total, delta_rows, score_scale, key_all, value_all
    )
    grad_key_own = rings.ctx_scatter_rows(grad_keys.reshape(-1, width_all))
    grad_value_own = rings.ctx_scatter_rows(grad_values.reshape(-1, width_all))
    grad_projected = jnp.concatenate(
        [
            grad_query.reshape(row_count, width_all),
            grad_key_own,
            grad_value_own,
        ],
        axis=1,
    ).astype(jnp.bfloat16)
    grad_in = weight_grad(normed_one_low, grad_projected, input_proj.shape[0])
    grad_normed_one = jnp.einsum(
        "re,de->rd", grad_projected, proj_in, preferred_element_type=jnp.float32
    )
    grad_hidden_norm, grad_gain_one, grad_shift_one = norm_pull_one(grad_normed_one)
    grad_hidden = grad_after + grad_hidden_norm
    grad_types = jnp.einsum("rt,rd->td", onehot, grad_hidden, precision=lax.Precision.HIGHEST)

    small_grads = jnp.concatenate(
        [
            jnp.stack(
                [
                    grad_gain_one,
                    grad_shift_one,
                    grad_out_bias,
                    grad_gain_two,
                    grad_shift_two,
                    grad_down_bias,
                ],
                axis=1,
            ),
            grad_types.T,
            grad_up_bias.reshape(width_all, ff_per_row),
            jnp.broadcast_to(local_square, (width_all, 1)),
        ],
        axis=1,
    )
    small_width = small_grads.shape[1]

    def small_block(b):
        shaped = small_grads.reshape(n_dp, n_ctx, shard_rows, small_width)
        return lax.dynamic_index_in_dim(shaped, b, 1, keepdims=False).reshape(
            n_dp * shard_rows, small_width
        )

    small_own = rings.scatter(
        small_block, shard_rows, small_width, colors=1, send_dtype=jnp.float32
    )
    loss_value = small_own[0, -1] / (valid_total * width_all)
    owned_gain_one, owned_shift_one, owned_out_bias, owned_gain_two, owned_shift_two = (
        small_own[:, k] for k in range(5)
    )
    owned_down_bias = small_own[:, 5]
    owned_types = small_own[:, 6 : 6 + TYPES].T
    owned_up_bias = small_own[:, 6 + TYPES : 6 + TYPES + ff_per_row].reshape(-1)
    return (
        result.reshape(batch_size, tok_rows, width_all),
        loss_value,
        grad_hidden.reshape(batch_size, tok_rows, width_all),
        owned_types,
        owned_gain_one,
        owned_shift_one,
        grad_in,
        grad_out,
        owned_out_bias,
        owned_gain_two,
        owned_shift_two,
        grad_up,
        owned_up_bias,
        grad_down,
        owned_down_bias,
    )


def solution(mesh):
    subs = dp_subaxes(mesh)

    def step(*args):
        return body(subs, *args)

    return jax.shard_map(
        step,
        mesh=mesh,
        in_specs=(
            P("dp", "ctx", None),
            P("dp", "ctx", None),
            P("dp", "ctx"),
            P("dp", "ctx"),
            P(None, ("dp", "ctx")),
            P(("dp", "ctx")),
            P(("dp", "ctx")),
            P(("dp", "ctx"), None),
            P(("dp", "ctx"), None),
            P(("dp", "ctx")),
            P(("dp", "ctx")),
            P(("dp", "ctx")),
            P(("dp", "ctx"), None),
            P(("dp", "ctx")),
            P(("dp", "ctx"), None),
            P(("dp", "ctx")),
        ),
        out_specs=(
            P("dp", "ctx", None),
            P(),
            P("dp", "ctx", None),
            P(None, ("dp", "ctx")),
            P(("dp", "ctx")),
            P(("dp", "ctx")),
            P(("dp", "ctx"), None),
            P(("dp", "ctx"), None),
            P(("dp", "ctx")),
            P(("dp", "ctx")),
            P(("dp", "ctx")),
            P(("dp", "ctx"), None),
            P(("dp", "ctx")),
            P(("dp", "ctx"), None),
            P(("dp", "ctx")),
        ),
        check_vma=False,
    )
```
